32 devices in a mesh: user: 8 (over z, y), item: 4 (over x, core).
Axes of the slice: x: 2, y: 2, z: 4, core: 2. Of those that a mesh axis runs over, the one named last changes fastest.
Arguments:
- theta_shape: float32 [16384, 1024], P('user', 'item'), may hold values from 0.3 to 3
- theta_rate: float32 [16384, 1024], P('user', 'item'), may hold values from 100 to 1000
- xi_rate: float32 [16384], P('user'), may hold values from 1 to 10
- beta_shape: float32 [4096, 1024], P('item', 'user'), may hold values from 0.3 to 3
- beta_rate: float32 [4096, 1024], P('item', 'user'), may hold values from 50 to 500
- eta_rate: float32 [4096], P('item'), may hold values from 1 to 10
- tile_slots: int32 [8, 4, 32], P('user', 'item'), may hold values from 0 to 31, as said below
- tile_counts: bfloat16 [8, 4, 32, 256, 256], P('user', 'item'), may hold values from 0 to 5, as said below
- live_tiles: int32 [8, 4], P('user', 'item'), may hold values from 1 to 32, as said below
Outputs:
- theta_shape_new: float32 [16384, 1024], P('user', 'item')
- theta_log_rate: float32 [16384, 1024], P('user', 'item')
- xi_rate_new: float32 [16384], P('user')
- beta_shape_new: float32 [4096, 1024], P('item', 'user')
- beta_log_rate: float32 [4096, 1024], P('item', 'user')
- eta_rate_new: float32 [4096], P('item')
The draws below stay inside these ranges and needn't reach their ends.
Inputs may be any that keep to these rules, and one draw needn't show every extreme that they name: `tile_slots`: within one device's 32 slots the positions are distinct. `tile_counts`: whole numbers. `live_tiles`: some device uses all 32 slots.
All inputs are finite; a program needn't handle non-finite values.
Results may differ from the reference program's by a relative error of at most 0.0029.
Values may be sent and summed in bfloat16 or wider, within the bound.
No kernel may reach another device: no remote copies, remote signals or barrier semaphores. Data moves between devices by JAX's collectives and lax.ppermute only.
A program may use at most 128 MiB of HBM per device.

```python
import math
import jax
import jax.numpy as jnp
from jax import lax

K = 1024
BLK = 256
UB = 8
IB = 4
TMAX = 32
NU = 16384
NI = 4096
N_USER = 8
N_ITEM = 4


def draw_tile_slots(key, part):
    device_keys = jax.random.split(key, N_USER * N_ITEM)
    orders = jax.vmap(lambda device_key: jax.random.permutation(device_key, UB * IB))(device_keys)
    return orders[:, :TMAX].reshape(N_USER, N_ITEM, TMAX).astype(jnp.int32)


def draw_tile_counts(key, part):
    values = jax.random.randint(key, (N_USER, N_ITEM, TMAX, BLK, BLK), 0, 6)
    return values.astype(jnp.float32).astype(jnp.bfloat16)


def draw_live_tiles(key, part):
    key_rank = jax.random.fold_in(key, 11)
    key_chosen = jax.random.fold_in(key, 23)
    ranked = jax.random.randint(key_rank, (N_USER * N_ITEM,), 1, TMAX + 1)
    loaded = jnp.maximum(1, ranked * ranked // TMAX)
    chosen = jax.random.randint(key_chosen, (), 0, N_USER * N_ITEM)
    loaded = jnp.where(jnp.arange(N_USER * N_ITEM) == chosen, TMAX, loaded)
    return loaded.reshape(N_USER, N_ITEM).astype(jnp.int32)


def block_levels(stream_key, extent, pieces, smallest, top_value):
    loudness, own = 1.0, jax.random.fold_in(stream_key, 6)
    for axis_at, shards_of in pieces:
        heights = jnp.exp(jax.random.uniform(jax.random.fold_in(own, axis_at), (shards_of,), jnp.float32, smallest / len(pieces), top_value / len(pieces)))
        loudness = loudness * jnp.repeat(heights, extent[axis_at] // shards_of).reshape([-1 if axis == axis_at else 1 for axis in range(len(extent))])
    return loudness


def setup_inputs(seed: int = 0) -> dict:
    keys = jax.random.split(jax.random.key(seed), 10)
    return {
        "theta_shape": jnp.clip(jnp.exp(math.log(3.0) - 2.3025851 * jax.random.uniform(keys[0], (NU, K), jnp.float32) ** block_levels(keys[0], (NU, K), ((0, 8), (1, 4)), -0.2, 0.2)), 0.3, 3.0),
        "theta_rate": jnp.clip(jnp.exp(math.log(1000.0) - 2.3025851 * jax.random.uniform(keys[1], (NU, K), jnp.float32) ** block_levels(keys[1], (NU, K), ((0, 8), (1, 4)), -0.2, 0.2)), 100.0, 1000.0),
        "xi_rate": jnp.clip(jnp.exp(math.log(10.0) - 2.3025851 * jax.random.uniform(keys[2], (NU,), jnp.float32) ** block_levels(keys[2], (NU,), ((0, 8),), -0.2, 0.2)), 1.0, 10.0),
        "beta_shape": jnp.clip(jnp.exp(math.log(3.0) - 2.3025851 * jax.random.uniform(keys[3], (NI, K), jnp.float32) ** block_levels(keys[3], (NI, K), ((0, 4), (1, 8)), -0.2, 0.2)), 0.3, 3.0),
        "beta_rate": jnp.clip(jnp.exp(math.log(500.0) - 2.3025851 * jax.random.uniform(keys[4], (NI, K), jnp.float32) ** block_levels(keys[4], (NI, K), ((0, 4), (1, 8)), -0.2, 0.2)), 50.0, 500.0),
        "eta_rate": jnp.clip(jnp.exp(math.log(10.0) - 2.3025851 * jax.random.uniform(keys[5], (NI,), jnp.float32) ** block_levels(keys[5], (NI,), ((0, 4),), -0.2, 0.2)), 1.0, 10.0),
        "tile_slots": draw_tile_slots(jax.random.fold_in(keys[9], 71), 0),
        "tile_counts": draw_tile_counts(jax.random.fold_in(keys[9], 71), 0),
        "live_tiles": draw_live_tiles(jax.random.fold_in(keys[9], 71), 0),
    }


prior_a = 0.3
prior_a2 = 0.3
prior_b2 = 1.0
prior_c = 0.3
prior_c2 = 0.3
prior_d2 = 1.0


def exp_mean_log(shape_param, rate_param):
    return jnp.exp(lax.digamma(shape_param) - jnp.log(rate_param)).astype(jnp.bfloat16)


def reference(theta_shape, theta_rate, xi_rate, beta_shape, beta_rate, eta_rate, tile_slots, tile_counts, live_tiles):
    theta_exp = exp_mean_log(theta_shape, theta_rate)
    beta_exp = exp_mean_log(beta_shape, beta_rate)

    def device_step(device, accum):
        row_shard = (device // N_ITEM).astype(jnp.int32)
        col_shard = (device % N_ITEM).astype(jnp.int32)
        slot_list = tile_slots[row_shard, col_shard]

        def tile_step(slot, inner):
            user_acc, item_acc = inner
            position = slot_list[slot]
            user_start = ((row_shard * UB + position // IB) * BLK).astype(jnp.int32)
            item_start = ((col_shard * IB + position % IB) * BLK).astype(jnp.int32)
            users = lax.dynamic_slice_in_dim(theta_exp, user_start, BLK, 0)
            items = lax.dynamic_slice_in_dim(beta_exp, item_start, BLK, 0)
            counts = tile_counts[row_shard, col_shard, slot].astype(jnp.float32)
            denominator = jnp.dot(users, items.T, preferred_element_type=jnp.float32)
            ratio_tile = (counts / denominator).astype(jnp.bfloat16)
            user_terms = jnp.dot(ratio_tile, items, preferred_element_type=jnp.float32)
            item_terms = jnp.dot(ratio_tile.T, users, preferred_element_type=jnp.float32)
            old_user = lax.dynamic_slice_in_dim(user_acc, user_start, BLK, 0)
            old_item = lax.dynamic_slice_in_dim(item_acc, item_start, BLK, 0)
            user_acc = lax.dynamic_update_slice_in_dim(user_acc, old_user + user_terms, user_start, 0)
            item_acc = lax.dynamic_update_slice_in_dim(item_acc, old_item + item_terms, item_start, 0)
            return (user_acc, item_acc)

        return lax.fori_loop(0, live_tiles[row_shard, col_shard], tile_step, accum)

    start_acc = (jnp.zeros((NU, K), jnp.float32), jnp.zeros((NI, K), jnp.float32))
    user_sum, item_sum = lax.fori_loop(0, N_USER * N_ITEM, device_step, start_acc)

    beta_total = jnp.sum(beta_shape / beta_rate, axis=0)
    theta_total = jnp.sum(theta_shape / theta_rate, axis=0)

    theta_shape_new = prior_a + theta_exp.astype(jnp.float32) * user_sum
    theta_rate_new = ((prior_a2 + K * prior_a) / xi_rate)[:, None] + beta_total[None, :]
    xi_rate_new = prior_a2 / prior_b2 + jnp.sum(theta_shape_new / theta_rate_new, axis=1)

    beta_shape_new = prior_c + beta_exp.astype(jnp.float32) * item_sum
    beta_rate_new = ((prior_c2 + K * prior_c) / eta_rate)[:, None] + theta_total[None, :]
    eta_rate_new = prior_c2 / prior_d2 + jnp.sum(beta_shape_new / beta_rate_new, axis=1)

    return (theta_shape_new, jnp.log(theta_rate_new), xi_rate_new, beta_shape_new, jnp.log(beta_rate_new), eta_rate_new)
```

```python
import jax
import jax.numpy as jnp
from jax import lax
from jax.sharding import PartitionSpec as P

BLK = 256
UB = 8
IB = 4
TMAX = 32


prior_a = 0.3
prior_a2 = 0.3
prior_b2 = 1.0
prior_c = 0.3
prior_c2 = 0.3
prior_d2 = 1.0


def exp_mean_log(shape_param, rate_param):
    return jnp.exp(lax.digamma(shape_param) - jnp.log(rate_param)).astype(jnp.bfloat16)


def dense_counts(tile_slots, tile_counts, live_tiles):
    slot_list = tile_slots.reshape(TMAX)
    used_slots = live_tiles.reshape(())
    positions = jnp.arange(UB * IB, dtype=jnp.int32)
    live = jnp.arange(TMAX, dtype=jnp.int32) < used_slots
    match = (slot_list[None, :] == positions[:, None]) & live[None, :]
    present = jnp.any(match, axis=1)
    source = jnp.argmax(match, axis=1)
    count_tiles = tile_counts.reshape(TMAX, BLK, BLK)
    grid = jnp.take(count_tiles, source, axis=0)
    grid = jnp.where(present[:, None, None], grid, jnp.zeros_like(grid))
    return grid.reshape(UB, IB, BLK, BLK)


def on_device(
    theta_shape,
    theta_rate,
    xi_rate,
    beta_shape,
    beta_rate,
    eta_rate,
    tile_slots,
    tile_counts,
    live_tiles,
):
    user_width = lax.axis_size("user")
    item_width = lax.axis_size("item")
    user_index = lax.axis_index("user")
    item_index = lax.axis_index("item")
    theta_part = exp_mean_log(theta_shape, theta_rate)
    beta_part = exp_mean_log(beta_shape, beta_rate)
    theta_full = lax.all_gather(theta_part, "item", axis=1, tiled=True)
    beta_full = lax.all_gather(beta_part, "user", axis=1, tiled=True)
    factors = theta_full.shape[1]
    user_rows = theta_full.shape[0]
    item_rows = beta_full.shape[0]
    theta_blocks = theta_full.reshape(UB, BLK, factors)
    beta_blocks = beta_full.reshape(IB, BLK, factors)
    counts = dense_counts(tile_slots, tile_counts, live_tiles).astype(jnp.float32)
    denominator = jnp.einsum(
        "buk,jik->bjui", theta_blocks, beta_blocks, preferred_element_type=jnp.float32
    )
    ratio = (counts / denominator).astype(jnp.bfloat16)
    user_acc = jnp.einsum("bjui,jik->buk", ratio, beta_blocks, preferred_element_type=jnp.float32)
    item_acc = jnp.einsum("bjui,buk->jik", ratio, theta_blocks, preferred_element_type=jnp.float32)
    user_acc = user_acc.reshape(user_rows, factors)
    item_acc = item_acc.reshape(item_rows, factors)
    beta_columns = factors // user_width
    theta_columns = factors // item_width
    beta_local = jnp.sum(beta_shape / beta_rate, axis=0)
    theta_local = jnp.sum(theta_shape / theta_rate, axis=0)
    beta_placed = lax.dynamic_update_slice_in_dim(
        jnp.zeros((factors,), jnp.float32), beta_local, user_index * beta_columns, 0
    )
    theta_placed = lax.dynamic_update_slice_in_dim(
        jnp.zeros((factors,), jnp.float32), theta_local, item_index * theta_columns, 0
    )
    beta_total, theta_total = lax.psum((beta_placed, theta_placed), ("user", "item"))
    xi_mean = (prior_a2 + factors * prior_a) / xi_rate
    user_share = lax.psum_scatter(user_acc, "item", scatter_dimension=1, tiled=True)
    theta_shape_new = prior_a + theta_part.astype(jnp.float32) * user_share
    beta_slice = lax.dynamic_slice_in_dim(beta_total, item_index * theta_columns, theta_columns, 0)
    theta_rate_new = xi_mean[:, None] + beta_slice[None, :]
    user_part = jnp.sum(theta_shape_new / theta_rate_new, axis=1)
    xi_rate_new = prior_a2 / prior_b2 + lax.psum(user_part, "item")
    item_share = lax.psum_scatter(item_acc, "user", scatter_dimension=1, tiled=True)
    beta_shape_new = prior_c + beta_part.astype(jnp.float32) * item_share
    eta_mean = (prior_c2 + factors * prior_c) / eta_rate
    theta_slice = lax.dynamic_slice_in_dim(theta_total, user_index * beta_columns, beta_columns, 0)
    beta_rate_new = eta_mean[:, None] + theta_slice[None, :]
    item_part = jnp.sum(beta_shape_new / beta_rate_new, axis=1)
    eta_rate_new = prior_c2 / prior_d2 + lax.psum(item_part, "user")
    return (
        theta_shape_new,
        jnp.log(theta_rate_new),
        xi_rate_new,
        beta_shape_new,
        jnp.log(beta_rate_new),
        eta_rate_new,
    )


def solution(mesh):
    in_specs = (
        P("user", "item"),
        P("user", "item"),
        P("user"),
        P("item", "user"),
        P("item", "user"),
        P("item"),
        P("user", "item", None),
        P("user", "item", None, None, None),
        P("user", "item"),
    )
    out_specs = (
        P("user", "item"),
        P("user", "item"),
        P("user"),
        P("item", "user"),
        P("item", "user"),
        P("item"),
    )
    return jax.shard_map(
        on_device, mesh=mesh, in_specs=in_specs, out_specs=out_specs, check_vma=False
    )
```

```python
import jax
import jax.numpy as jnp
from jax import lax
from jax.sharding import PartitionSpec as P

BLK = 256
UB = 8
IB = 4
TMAX = 32


prior_a = 0.3
prior_a2 = 0.3
prior_b2 = 1.0
prior_c = 0.3
prior_c2 = 0.3
prior_d2 = 1.0


def exp_mean_log(shape_param, rate_param):
    return jnp.exp(lax.digamma(shape_param) - jnp.log(rate_param)).astype(jnp.bfloat16)


def dense_counts(tile_slots, tile_counts, live_tiles):
    slot_list = tile_slots.reshape(TMAX)
    used_slots = live_tiles.reshape(())
    positions = jnp.arange(UB * IB, dtype=jnp.int32)
    live = jnp.arange(TMAX, dtype=jnp.int32) < used_slots
    match = (slot_list[None, :] == positions[:, None]) & live[None, :]
    present = jnp.any(match, axis=1)
    source = jnp.argmax(match, axis=1)
    count_tiles = tile_counts.reshape(TMAX, BLK, BLK)
    grid = jnp.take(count_tiles, source, axis=0)
    grid = jnp.where(present[:, None, None], grid, jnp.zeros_like(grid))
    return grid.reshape(UB, IB, BLK, BLK)


def on_device(
    theta_shape,
    theta_rate,
    xi_rate,
    beta_shape,
    beta_rate,
    eta_rate,
    tile_slots,
    tile_counts,
    live_tiles,
):
    user_width = lax.axis_size("user")
    item_width = lax.axis_size("item")
    user_index = lax.axis_index("user")
    item_index = lax.axis_index("item")
    factors = theta_shape.shape[1] * item_width
    beta_columns = factors // user_width
    theta_columns = factors // item_width
    theta_part = exp_mean_log(theta_shape, theta_rate)
    beta_part = exp_mean_log(beta_shape, beta_rate)
    beta_local = jnp.sum(beta_shape / beta_rate, axis=0)
    theta_local = jnp.sum(theta_shape / theta_rate, axis=0)
    beta_placed = lax.dynamic_update_slice_in_dim(
        jnp.zeros((factors,), jnp.float32), beta_local, user_index * beta_columns, 0
    )
    theta_placed = lax.dynamic_update_slice_in_dim(
        jnp.zeros((factors,), jnp.float32), theta_local, item_index * theta_columns, 0
    )
    theta_full = lax.all_gather(theta_part, "item", axis=1, tiled=True)
    beta_full = lax.all_gather(beta_part, "user", axis=1, tiled=True)
    theta_part, beta_placed, theta_placed = lax.optimization_barrier(
        (theta_part, beta_placed, theta_placed)
    )
    beta_total, theta_total = lax.psum((beta_placed, theta_placed), ("user", "item"))
    tile_counts, beta_total, theta_total = lax.optimization_barrier(
        (tile_counts, beta_total, theta_total)
    )
    user_rows = theta_full.shape[0]
    item_rows = beta_full.shape[0]
    theta_blocks = theta_full.reshape(UB, BLK, factors)
    beta_blocks = beta_full.reshape(IB, BLK, factors)
    counts = dense_counts(tile_slots, tile_counts, live_tiles).astype(jnp.float32)
    denominator = jnp.einsum(
        "buk,jik->bjui", theta_blocks, beta_blocks, preferred_element_type=jnp.float32
    )
    ratio = (counts / denominator).astype(jnp.bfloat16)
    user_acc = jnp.einsum("bjui,jik->buk", ratio, beta_blocks, preferred_element_type=jnp.float32)
    item_acc = jnp.einsum("bjui,buk->jik", ratio, theta_blocks, preferred_element_type=jnp.float32)
    user_acc = user_acc.reshape(user_rows, factors)
    item_acc = item_acc.reshape(item_rows, factors)
    xi_mean = (prior_a2 + factors * prior_a) / xi_rate
    user_share = lax.psum_scatter(user_acc, "item", scatter_dimension=1, tiled=True)
    theta_shape_new = prior_a + theta_part.astype(jnp.float32) * user_share
    beta_slice = lax.dynamic_slice_in_dim(beta_total, item_index * theta_columns, theta_columns, 0)
    theta_rate_new = xi_mean[:, None] + beta_slice[None, :]
    user_part = jnp.sum(theta_shape_new / theta_rate_new, axis=1)
    xi_rate_new = prior_a2 / prior_b2 + lax.psum(user_part, "item")
    item_share = lax.psum_scatter(item_acc, "user", scatter_dimension=1, tiled=True)
    beta_shape_new = prior_c + beta_part.astype(jnp.float32) * item_share
    eta_mean = (prior_c2 + factors * prior_c) / eta_rate
    theta_slice = lax.dynamic_slice_in_dim(theta_total, user_index * beta_columns, beta_columns, 0)
    beta_rate_new = eta_mean[:, None] + theta_slice[None, :]
    item_part = jnp.sum(beta_shape_new / beta_rate_new, axis=1)
    eta_rate_new = prior_c2 / prior_d2 + lax.psum(item_part, "user")
    return (
        theta_shape_new,
        jnp.log(theta_rate_new),
        xi_rate_new,
        beta_shape_new,
        jnp.log(beta_rate_new),
        eta_rate_new,
    )


def solution(mesh):
    in_specs = (
        P("user", "item"),
        P("user", "item"),
        P("user"),
        P("item", "user"),
        P("item", "user"),
        P("item"),
        P("user", "item", None),
        P("user", "item", None, None, None),
        P("user", "item"),
    )
    out_specs = (
        P("user", "item"),
        P("user", "item"),
        P("user"),
        P("item", "user"),
        P("item", "user"),
        P("item"),
    )
    return jax.shard_map(
        on_device, mesh=mesh, in_specs=in_specs, out_specs=out_specs, check_vma=False
    )
```

```python
import jax
import jax.numpy as jnp
from jax import lax
from jax.sharding import PartitionSpec as P

BLK = 256
UB = 8
IB = 4
TMAX = 32


prior_a = 0.3
prior_a2 = 0.3
prior_b2 = 1.0
prior_c = 0.3
prior_c2 = 0.3
prior_d2 = 1.0


def exp_mean_log(shape_param, rate_param):
    return jnp.exp(lax.digamma(shape_param) - jnp.log(rate_param)).astype(jnp.bfloat16)


def dense_counts(tile_slots, tile_counts, live_tiles):
    slot_list = tile_slots.reshape(TMAX)
    used_slots = live_tiles.reshape(())
    positions = jnp.arange(UB * IB, dtype=jnp.int32)
    live = jnp.arange(TMAX, dtype=jnp.int32) < used_slots
    match = (slot_list[None, :] == positions[:, None]) & live[None, :]
    present = jnp.any(match, axis=1)
    source = jnp.argmax(match, axis=1)
    count_tiles = tile_counts.reshape(TMAX, BLK, BLK)
    grid = jnp.take(count_tiles, source, axis=0)
    grid = jnp.where(present[:, None, None], grid, jnp.zeros_like(grid))
    return grid.reshape(UB, IB, BLK, BLK)


def halving_reduce_scatter(partial, axis_name, width, index):
    rows, columns = partial.shape
    block = columns // width
    held = partial.reshape(rows, width, block)
    bit = 0
    while (1 << bit) < width:
        groups = held.shape[1] // 2
        pairs = held.reshape(rows, groups, 2, block)
        own_bit = (index >> bit) & 1
        keep = lax.dynamic_index_in_dim(pairs, own_bit, axis=2, keepdims=False)
        send = lax.dynamic_index_in_dim(pairs, 1 - own_bit, axis=2, keepdims=False)
        step = 1 << bit
        perm = [(i, i ^ step) for i in range(width)]
        held = keep + lax.ppermute(send, axis_name, perm)
        bit += 1
    return held.reshape(rows, block)


def on_device(
    theta_shape,
    theta_rate,
    xi_rate,
    beta_shape,
    beta_rate,
    eta_rate,
    tile_slots,
    tile_counts,
    live_tiles,
):
    user_width = lax.axis_size("user")
    item_width = lax.axis_size("item")
    user_index = lax.axis_index("user")
    item_index = lax.axis_index("item")
    factors = theta_shape.shape[1] * item_width
    beta_columns = factors // user_width
    theta_columns = factors // item_width
    theta_part = exp_mean_log(theta_shape, theta_rate)
    beta_part = exp_mean_log(beta_shape, beta_rate)
    beta_local = jnp.sum(beta_shape / beta_rate, axis=0)
    theta_local = jnp.sum(theta_shape / theta_rate, axis=0)
    beta_placed = lax.dynamic_update_slice_in_dim(
        jnp.zeros((factors,), jnp.float32), beta_local, user_index * beta_columns, 0
    )
    theta_placed = lax.dynamic_update_slice_in_dim(
        jnp.zeros((factors,), jnp.float32), theta_local, item_index * theta_columns, 0
    )
    theta_full = lax.all_gather(theta_part, "item", axis=1, tiled=True)
    beta_full = lax.all_gather(beta_part, "user", axis=1, tiled=True)
    theta_part, beta_placed, theta_placed = lax.optimization_barrier(
        (theta_part, beta_placed, theta_placed)
    )
    beta_total, theta_total = lax.psum((beta_placed, theta_placed), ("user", "item"))
    tile_counts, beta_total, theta_total = lax.optimization_barrier(
        (tile_counts, beta_total, theta_total)
    )
    user_rows = theta_full.shape[0]
    item_rows = beta_full.shape[0]
    theta_blocks = theta_full.reshape(UB, BLK, factors)
    beta_blocks = beta_full.reshape(IB, BLK, factors)
    counts = dense_counts(tile_slots, tile_counts, live_tiles).astype(jnp.float32)
    denominator = jnp.einsum(
        "buk,jik->bjui", theta_blocks, beta_blocks, preferred_element_type=jnp.float32
    )
    ratio = (counts / denominator).astype(jnp.bfloat16)
    user_acc = jnp.einsum("bjui,jik->buk", ratio, beta_blocks, preferred_element_type=jnp.float32)
    item_acc = jnp.einsum("bjui,buk->jik", ratio, theta_blocks, preferred_element_type=jnp.float32)
    user_acc = user_acc.reshape(user_rows, factors)
    item_acc = item_acc.reshape(item_rows, factors)
    xi_mean = (prior_a2 + factors * prior_a) / xi_rate
    user_share = halving_reduce_scatter(user_acc, "item", item_width, item_index)
    theta_shape_new = prior_a + theta_part.astype(jnp.float32) * user_share
    beta_slice = lax.dynamic_slice_in_dim(beta_total, item_index * theta_columns, theta_columns, 0)
    theta_rate_new = xi_mean[:, None] + beta_slice[None, :]
    user_part = jnp.sum(theta_shape_new / theta_rate_new, axis=1)
    xi_rate_new = prior_a2 / prior_b2 + lax.psum(user_part, "item")
    item_share = lax.psum_scatter(item_acc, "user", scatter_dimension=1, tiled=True)
    beta_shape_new = prior_c + beta_part.astype(jnp.float32) * item_share
    eta_mean = (prior_c2 + factors * prior_c) / eta_rate
    theta_slice = lax.dynamic_slice_in_dim(theta_total, user_index * beta_columns, beta_columns, 0)
    beta_rate_new = eta_mean[:, None] + theta_slice[None, :]
    item_part = jnp.sum(beta_shape_new / beta_rate_new, axis=1)
    eta_rate_new = prior_c2 / prior_d2 + lax.psum(item_part, "user")
    return (
        theta_shape_new,
        jnp.log(theta_rate_new),
        xi_rate_new,
        beta_shape_new,
        jnp.log(beta_rate_new),
        eta_rate_new,
    )


def solution(mesh):
    in_specs = (
        P("user", "item"),
        P("user", "item"),
        P("user"),
        P("item", "user"),
        P("item", "user"),
        P("item"),
        P("user", "item", None),
        P("user", "item", None, None, None),
        P("user", "item"),
    )
    out_specs = (
        P("user", "item"),
        P("user", "item"),
        P("user"),
        P("item", "user"),
        P("item", "user"),
        P("item"),
    )
    return jax.shard_map(
        on_device, mesh=mesh, in_specs=in_specs, out_specs=out_specs, check_vma=False
    )
```

```python
import jax
import jax.numpy as jnp
from jax import lax
from jax.sharding import PartitionSpec as P

BLK = 256
UB = 8
IB = 4
TMAX = 32


prior_a = 0.3
prior_a2 = 0.3
prior_b2 = 1.0
prior_c = 0.3
prior_c2 = 0.3
prior_d2 = 1.0


def exp_mean_log(shape_param, rate_param):
    return jnp.exp(lax.digamma(shape_param) - jnp.log(rate_param)).astype(jnp.bfloat16)


def dense_counts(tile_slots, tile_counts, live_tiles):
    slot_list = tile_slots.reshape(TMAX)
    used_slots = live_tiles.reshape(())
    positions = jnp.arange(UB * IB, dtype=jnp.int32)
    live = jnp.arange(TMAX, dtype=jnp.int32) < used_slots
    match = (slot_list[None, :] == positions[:, None]) & live[None, :]
    present = jnp.any(match, axis=1)
    source = jnp.argmax(match, axis=1)
    count_tiles = tile_counts.reshape(TMAX, BLK, BLK)
    grid = jnp.take(count_tiles, source, axis=0)
    grid = jnp.where(present[:, None, None], grid, jnp.zeros_like(grid))
    return grid.reshape(UB, IB, BLK, BLK)


def halving_order(width):
    order = [0]
    step = width
    while step > 1:
        step //= 2
        order = [c ^ step for c in order] + order
    return order


def halving_user_sums(ratio, beta_full, width, index, axis_name):
    items, factors = beta_full.shape
    block = factors // width
    order = jnp.asarray(halving_order(width), jnp.int32) ^ index
    beta_ordered = jnp.take(beta_full.reshape(items, width, block), order, axis=1)
    sizes = []
    size = width
    while size > 1:
        size //= 2
        sizes.append(size)
    sizes.append(1)
    terms = []
    first = 0
    for size in sizes:
        piece = beta_ordered[:, first : first + size].reshape(items, size * block)
        terms.append(jnp.dot(ratio, piece, preferred_element_type=jnp.float32))
        first += size
    for step_index in range(len(sizes) - 1):
        partner = 1 << step_index
        perm = [(i, i ^ partner) for i in range(width)]
        received = lax.ppermute(terms[step_index], axis_name, perm)
        offset = 0
        for later in range(step_index + 1, len(sizes)):
            span = terms[later].shape[1]
            terms[later] = terms[later] + received[:, offset : offset + span]
            offset += span
    return terms[-1]


def on_device(
    theta_shape,
    theta_rate,
    xi_rate,
    beta_shape,
    beta_rate,
    eta_rate,
    tile_slots,
    tile_counts,
    live_tiles,
):
    user_width = lax.axis_size("user")
    item_width = lax.axis_size("item")
    user_index = lax.axis_index("user")
    item_index = lax.axis_index("item")
    factors = theta_shape.shape[1] * item_width
    beta_columns = factors // user_width
    theta_columns = factors // item_width
    theta_part = exp_mean_log(theta_shape, theta_rate)
    beta_part = exp_mean_log(beta_shape, beta_rate)
    beta_local = jnp.sum(beta_shape / beta_rate, axis=0)
    theta_local = jnp.sum(theta_shape / theta_rate, axis=0)
    beta_placed = lax.dynamic_update_slice_in_dim(
        jnp.zeros((factors,), jnp.float32), beta_local, user_index * beta_columns, 0
    )
    theta_placed = lax.dynamic_update_slice_in_dim(
        jnp.zeros((factors,), jnp.float32), theta_local, item_index * theta_columns, 0
    )
    theta_full = lax.all_gather(theta_part, "item", axis=1, tiled=True)
    beta_full = lax.all_gather(beta_part, "user", axis=1, tiled=True)
    theta_part, beta_placed, theta_placed = lax.optimization_barrier(
        (theta_part, beta_placed, theta_placed)
    )
    beta_total, theta_total = lax.psum((beta_placed, theta_placed), ("user", "item"))
    tile_counts, beta_total, theta_total = lax.optimization_barrier(
        (tile_counts, beta_total, theta_total)
    )
    user_rows = theta_full.shape[0]
    item_rows = beta_full.shape[0]
    grid = dense_counts(tile_slots, tile_counts, live_tiles)
    counts = grid.transpose(0, 2, 1, 3).reshape(user_rows, item_rows).astype(jnp.float32)
    denominator = lax.dot_general(
        theta_full, beta_full, (((1,), (1,)), ((), ())), preferred_element_type=jnp.float32
    )
    ratio = (counts / denominator).astype(jnp.bfloat16)
    item_acc = lax.dot_general(
        ratio, theta_full, (((0,), (0,)), ((), ())), preferred_element_type=jnp.float32
    )
    xi_mean = (prior_a2 + factors * prior_a) / xi_rate
    user_share = halving_user_sums(ratio, beta_full, item_width, item_index, "item")
    theta_shape_new = prior_a + theta_part.astype(jnp.float32) * user_share
    beta_slice = lax.dynamic_slice_in_dim(beta_total, item_index * theta_columns, theta_columns, 0)
    theta_rate_new = xi_mean[:, None] + beta_slice[None, :]
    user_part = jnp.sum(theta_shape_new / theta_rate_new, axis=1)
    xi_rate_new = prior_a2 / prior_b2 + lax.psum(user_part, "item")
    item_share = lax.psum_scatter(item_acc, "user", scatter_dimension=1, tiled=True)
    beta_shape_new = prior_c + beta_part.astype(jnp.float32) * item_share
    eta_mean = (prior_c2 + factors * prior_c) / eta_rate
    theta_slice = lax.dynamic_slice_in_dim(theta_total, user_index * beta_columns, beta_columns, 0)
    beta_rate_new = eta_mean[:, None] + theta_slice[None, :]
    item_part = jnp.sum(beta_shape_new / beta_rate_new, axis=1)
    eta_rate_new = prior_c2 / prior_d2 + lax.psum(item_part, "user")
    return (
        theta_shape_new,
        jnp.log(theta_rate_new),
        xi_rate_new,
        beta_shape_new,
        jnp.log(beta_rate_new),
        eta_rate_new,
    )


def solution(mesh):
    in_specs = (
        P("user", "item"),
        P("user", "item"),
        P("user"),
        P("item", "user"),
        P("item", "user"),
        P("item"),
        P("user", "item", None),
        P("user", "item", None, None, None),
        P("user", "item"),
    )
    out_specs = (
        P("user", "item"),
        P("user", "item"),
        P("user"),
        P("item", "user"),
        P("item", "user"),
        P("item"),
    )
    return jax.shard_map(
        on_device, mesh=mesh, in_specs=in_specs, out_specs=out_specs, check_vma=False
    )
```

```python
import jax
import jax.numpy as jnp
from jax import lax
from jax.sharding import PartitionSpec as P

BLK = 256
UB = 8
IB = 4
TMAX = 32


prior_a = 0.3
prior_a2 = 0.3
prior_b2 = 1.0
prior_c = 0.3
prior_c2 = 0.3
prior_d2 = 1.0


def exp_mean_log(shape_param, rate_param):
    return jnp.exp(lax.digamma(shape_param) - jnp.log(rate_param)).astype(jnp.bfloat16)


def dense_counts(tile_slots, tile_counts, live_tiles):
    slot_list = tile_slots.reshape(TMAX)
    used_slots = live_tiles.reshape(())
    positions = jnp.arange(UB * IB, dtype=jnp.int32)
    live = jnp.arange(TMAX, dtype=jnp.int32) < used_slots
    match = (slot_list[None, :] == positions[:, None]) & live[None, :]
    present = jnp.any(match, axis=1)
    source = jnp.argmax(match, axis=1)
    count_tiles = tile_counts.reshape(TMAX, BLK, BLK)
    grid = jnp.take(count_tiles, source, axis=0)
    grid = jnp.where(present[:, None, None], grid, jnp.zeros_like(grid))
    return grid.reshape(UB, IB, BLK, BLK)


def doubling_gather(part, axis_name, width, index):
    rows, block = part.shape
    held = part.reshape(rows, 1, block)
    bit = width.bit_length() - 2
    while bit >= 0:
        partner = 1 << bit
        perm = [(i, i ^ partner) for i in range(width)]
        other = lax.ppermute(held, axis_name, perm)
        upper = ((index >> bit) & 1) == 1
        low = jnp.where(upper, other, held)
        high = jnp.where(upper, held, other)
        held = jnp.stack([low, high], axis=2).reshape(rows, 2 * held.shape[1], block)
        bit -= 1
    return held.reshape(rows, width * block)


def halving_order(width):
    order = [0]
    step = width
    while step > 1:
        step //= 2
        order = [c ^ step for c in order] + order
    return order


def halving_user_sums(ratio, beta_full, width, index, axis_name, extra):
    items, factors = beta_full.shape
    block = factors // width
    order = jnp.asarray(halving_order(width), jnp.int32) ^ index
    beta_ordered = jnp.take(beta_full.reshape(items, width, block), order, axis=1)
    sizes = []
    size = width
    while size > 1:
        size //= 2
        sizes.append(size)
    sizes.append(1)
    terms = []
    first = 0
    for size in sizes:
        piece = beta_ordered[:, first : first + size].reshape(items, size * block)
        terms.append(jnp.dot(ratio, piece, preferred_element_type=jnp.float32))
        first += size
    for step_index in range(len(sizes) - 1):
        partner = 1 << step_index
        perm = [(i, i ^ partner) for i in range(width)]
        if step_index == len(sizes) - 2:
            terms[step_index], extra = lax.optimization_barrier((terms[step_index], extra))
        received = lax.ppermute(terms[step_index], axis_name, perm)
        offset = 0
        for later in range(step_index + 1, len(sizes)):
            span = terms[later].shape[1]
            terms[later] = terms[later] + received[:, offset : offset + span]
            offset += span
    return terms[-1], extra


def on_device(
    theta_shape,
    theta_rate,
    xi_rate,
    beta_shape,
    beta_rate,
    eta_rate,
    tile_slots,
    tile_counts,
    live_tiles,
):
    user_width = lax.axis_size("user")
    item_width = lax.axis_size("item")
    user_index = lax.axis_index("user")
    item_index = lax.axis_index("item")
    factors = theta_shape.shape[1] * item_width
    beta_columns = factors // user_width
    theta_columns = factors // item_width
    theta_part = exp_mean_log(theta_shape, theta_rate)
    beta_part = exp_mean_log(beta_shape, beta_rate)
    beta_local = jnp.sum(beta_shape / beta_rate, axis=0)
    theta_local = jnp.sum(theta_shape / theta_rate, axis=0)
    beta_placed = lax.dynamic_update_slice_in_dim(
        jnp.zeros((factors,), jnp.float32), beta_local, user_index * beta_columns, 0
    )
    theta_placed = lax.dynamic_update_slice_in_dim(
        jnp.zeros((factors,), jnp.float32), theta_local, item_index * theta_columns, 0
    )
    theta_full = doubling_gather(theta_part, "item", item_width, item_index)
    beta_full = lax.all_gather(beta_part, "user", axis=1, tiled=True)
    user_rows = theta_full.shape[0]
    item_rows = beta_full.shape[0]
    grid = dense_counts(tile_slots, tile_counts, live_tiles)
    counts = grid.transpose(0, 2, 1, 3).reshape(user_rows, item_rows).astype(jnp.float32)
    denominator = lax.dot_general(
        theta_full, beta_full, (((1,), (1,)), ((), ())), preferred_element_type=jnp.float32
    )
    ratio = (counts / denominator).astype(jnp.bfloat16)
    item_acc = lax.dot_general(
        ratio, theta_full, (((0,), (0,)), ((), ())), preferred_element_type=jnp.float32
    )
    xi_mean = (prior_a2 + factors * prior_a) / xi_rate
    user_share, placed = halving_user_sums(
        ratio, beta_full, item_width, item_index, "item", (beta_placed, theta_placed)
    )
    beta_total, theta_total = lax.psum(placed, ("user", "item"))
    theta_shape_new = prior_a + theta_part.astype(jnp.float32) * user_share
    beta_slice = lax.dynamic_slice_in_dim(beta_total, item_index * theta_columns, theta_columns, 0)
    theta_rate_new = xi_mean[:, None] + beta_slice[None, :]
    user_part = jnp.sum(theta_shape_new / theta_rate_new, axis=1)
    xi_rate_new = prior_a2 / prior_b2 + lax.psum(user_part, "item")
    item_share = lax.psum_scatter(item_acc, "user", scatter_dimension=1, tiled=True)
    beta_shape_new = prior_c + beta_part.astype(jnp.float32) * item_share
    eta_mean = (prior_c2 + factors * prior_c) / eta_rate
    theta_slice = lax.dynamic_slice_in_dim(theta_total, user_index * beta_columns, beta_columns, 0)
    beta_rate_new = eta_mean[:, None] + theta_slice[None, :]
    item_part = jnp.sum(beta_shape_new / beta_rate_new, axis=1)
    eta_rate_new = prior_c2 / prior_d2 + lax.psum(item_part, "user")
    return (
        theta_shape_new,
        jnp.log(theta_rate_new),
        xi_rate_new,
        beta_shape_new,
        jnp.log(beta_rate_new),
        eta_rate_new,
    )


def solution(mesh):
    in_specs = (
        P("user", "item"),
        P("user", "item"),
        P("user"),
        P("item", "user"),
        P("item", "user"),
        P("item"),
        P("user", "item", None),
        P("user", "item", None, None, None),
        P("user", "item"),
    )
    out_specs = (
        P("user", "item"),
        P("user", "item"),
        P("user"),
        P("item", "user"),
        P("item", "user"),
        P("item"),
    )
    return jax.shard_map(
        on_device, mesh=mesh, in_specs=in_specs, out_specs=out_specs, check_vma=False
    )
```

```python
import jax
import jax.numpy as jnp
from jax import lax
from jax.sharding import PartitionSpec as P

BLK = 256
UB = 8
IB = 4
TMAX = 32


prior_a = 0.3
prior_a2 = 0.3
prior_b2 = 1.0
prior_c = 0.3
prior_c2 = 0.3
prior_d2 = 1.0


def exp_mean_log(shape_param, rate_param):
    return jnp.exp(lax.digamma(shape_param) - jnp.log(rate_param)).astype(jnp.bfloat16)


def dense_counts(tile_slots, tile_counts, live_tiles):
    slot_list = tile_slots.reshape(TMAX)
    used_slots = live_tiles.reshape(())
    positions = jnp.arange(UB * IB, dtype=jnp.int32)
    live = jnp.arange(TMAX, dtype=jnp.int32) < used_slots
    match = (slot_list[None, :] == positions[:, None]) & live[None, :]
    present = jnp.any(match, axis=1)
    source = jnp.argmax(match, axis=1)
    count_tiles = tile_counts.reshape(TMAX, BLK, BLK)
    grid = jnp.take(count_tiles, source, axis=0)
    grid = jnp.where(present[:, None, None], grid, jnp.zeros_like(grid))
    return grid.reshape(UB, IB, BLK, BLK)


def doubling_sum(value, axis_name, width):
    bit = 1
    while bit < width:
        perm = [(i, i ^ bit) for i in range(width)]
        value = value + lax.ppermute(value, axis_name, perm)
        bit *= 2
    return value


def doubling_gather(part, axis_name, width, index):
    rows, block = part.shape
    held = part.reshape(rows, 1, block)
    bit = width.bit_length() - 2
    while bit >= 0:
        partner = 1 << bit
        perm = [(i, i ^ partner) for i in range(width)]
        other = lax.ppermute(held, axis_name, perm)
        upper = ((index >> bit) & 1) == 1
        low = jnp.where(upper, other, held)
        high = jnp.where(upper, held, other)
        held = jnp.stack([low, high], axis=2).reshape(rows, 2 * held.shape[1], block)
        bit -= 1
    return held.reshape(rows, width * block)


def halving_order(width):
    order = [0]
    step = width
    while step > 1:
        step //= 2
        order = [c ^ step for c in order] + order
    return order


def halving_user_sums(ratio, beta_full, width, index, axis_name):
    items, factors = beta_full.shape
    block = factors // width
    order = jnp.asarray(halving_order(width), jnp.int32) ^ index
    beta_ordered = jnp.take(beta_full.reshape(items, width, block), order, axis=1)
    sizes = []
    size = width
    while size > 1:
        size //= 2
        sizes.append(size)
    sizes.append(1)
    terms = []
    first = 0
    for size in sizes:
        piece = beta_ordered[:, first : first + size].reshape(items, size * block)
        terms.append(jnp.dot(ratio, piece, preferred_element_type=jnp.float32))
        first += size
    for step_index in range(len(sizes) - 1):
        partner = 1 << step_index
        perm = [(i, i ^ partner) for i in range(width)]
        received = lax.ppermute(terms[step_index], axis_name, perm)
        offset = 0
        for later in range(step_index + 1, len(sizes)):
            span = terms[later].shape[1]
            terms[later] = terms[later] + received[:, offset : offset + span]
            offset += span
    return terms[-1]


def on_device(
    theta_shape,
    theta_rate,
    xi_rate,
    beta_shape,
    beta_rate,
    eta_rate,
    tile_slots,
    tile_counts,
    live_tiles,
):
    user_width = lax.axis_size("user")
    item_width = lax.axis_size("item")
    user_index = lax.axis_index("user")
    item_index = lax.axis_index("item")
    factors = theta_shape.shape[1] * item_width
    beta_columns = factors // user_width
    theta_columns = factors // item_width
    theta_part = exp_mean_log(theta_shape, theta_rate)
    beta_part = exp_mean_log(beta_shape, beta_rate)
    beta_local = jnp.sum(beta_shape / beta_rate, axis=0)
    theta_local = jnp.sum(theta_shape / theta_rate, axis=0)
    beta_placed = lax.dynamic_update_slice_in_dim(
        jnp.zeros((factors,), jnp.float32), beta_local, user_index * beta_columns, 0
    )
    theta_placed = lax.dynamic_update_slice_in_dim(
        jnp.zeros((factors,), jnp.float32), theta_local, item_index * theta_columns, 0
    )
    placed = jnp.stack([beta_placed, theta_placed])
    placed = doubling_sum(doubling_sum(placed, "item", item_width), "user", user_width)
    beta_total = placed[0]
    theta_total = placed[1]
    theta_full = doubling_gather(theta_part, "item", item_width, item_index)
    beta_full = lax.all_gather(beta_part, "user", axis=1, tiled=True)
    user_rows = theta_full.shape[0]
    item_rows = beta_full.shape[0]
    grid = dense_counts(tile_slots, tile_counts, live_tiles)
    counts = grid.transpose(0, 2, 1, 3).reshape(user_rows, item_rows).astype(jnp.float32)
    denominator = lax.dot_general(
        theta_full, beta_full, (((1,), (1,)), ((), ())), preferred_element_type=jnp.float32
    )
    ratio = (counts / denominator).astype(jnp.bfloat16)
    item_acc = lax.dot_general(
        ratio, theta_full, (((0,), (0,)), ((), ())), preferred_element_type=jnp.float32
    )
    xi_mean = (prior_a2 + factors * prior_a) / xi_rate
    user_share = halving_user_sums(ratio, beta_full, item_width, item_index, "item")
    theta_shape_new = prior_a + theta_part.astype(jnp.float32) * user_share
    beta_slice = lax.dynamic_slice_in_dim(beta_total, item_index * theta_columns, theta_columns, 0)
    theta_rate_new = xi_mean[:, None] + beta_slice[None, :]
    user_part = jnp.sum(theta_shape_new / theta_rate_new, axis=1)
    xi_rate_new = prior_a2 / prior_b2 + doubling_sum(user_part, "item", item_width)
    item_share = lax.psum_scatter(item_acc, "user", scatter_dimension=1, tiled=True)
    beta_shape_new = prior_c + beta_part.astype(jnp.float32) * item_share
    eta_mean = (prior_c2 + factors * prior_c) / eta_rate
    theta_slice = lax.dynamic_slice_in_dim(theta_total, user_index * beta_columns, beta_columns, 0)
    beta_rate_new = eta_mean[:, None] + theta_slice[None, :]
    item_part = jnp.sum(beta_shape_new / beta_rate_new, axis=1)
    eta_rate_new = prior_c2 / prior_d2 + doubling_sum(item_part, "user", user_width)
    return (
        theta_shape_new,
        jnp.log(theta_rate_new),
        xi_rate_new,
        beta_shape_new,
        jnp.log(beta_rate_new),
        eta_rate_new,
    )


def solution(mesh):
    in_specs = (
        P("user", "item"),
        P("user", "item"),
        P("user"),
        P("item", "user"),
        P("item", "user"),
        P("item"),
        P("user", "item", None),
        P("user", "item", None, None, None),
        P("user", "item"),
    )
    out_specs = (
        P("user", "item"),
        P("user", "item"),
        P("user"),
        P("item", "user"),
        P("item", "user"),
        P("item"),
    )
    return jax.shard_map(
        on_device, mesh=mesh, in_specs=in_specs, out_specs=out_specs, check_vma=False
    )
```

```python
import jax
import jax.numpy as jnp
from jax import lax
from jax.sharding import PartitionSpec as P

BLK = 256
UB = 8
IB = 4
TMAX = 32


prior_a = 0.3
prior_a2 = 0.3
prior_b2 = 1.0
prior_c = 0.3
prior_c2 = 0.3
prior_d2 = 1.0


def exp_mean_log(shape_param, rate_param):
    return jnp.exp(lax.digamma(shape_param) - jnp.log(rate_param)).astype(jnp.bfloat16)


def dense_counts(tile_slots, tile_counts, live_tiles):
    slot_list = tile_slots.reshape(TMAX)
    used_slots = live_tiles.reshape(())
    positions = jnp.arange(UB * IB, dtype=jnp.int32)
    live = jnp.arange(TMAX, dtype=jnp.int32) < used_slots
    match = (slot_list[None, :] == positions[:, None]) & live[None, :]
    present = jnp.any(match, axis=1)
    source = jnp.argmax(match, axis=1)
    count_tiles = tile_counts.reshape(TMAX, BLK, BLK)
    grid = jnp.take(count_tiles, source, axis=0)
    grid = jnp.where(present[:, None, None], grid, jnp.zeros_like(grid))
    return grid.reshape(UB, IB, BLK, BLK)


def doubling_sum(value, axis_name, width):
    bit = 1
    while bit < width:
        perm = [(i, i ^ bit) for i in range(width)]
        value = value + lax.ppermute(value, axis_name, perm)
        bit *= 2
    return value


def doubling_gather(part, axis_name, width, index):
    rows, block = part.shape
    held = part.reshape(rows, 1, block)
    bit = width.bit_length() - 2
    while bit >= 0:
        partner = 1 << bit
        perm = [(i, i ^ partner) for i in range(width)]
        other = lax.ppermute(held, axis_name, perm)
        upper = ((index >> bit) & 1) == 1
        low = jnp.where(upper, other, held)
        high = jnp.where(upper, held, other)
        held = jnp.stack([low, high], axis=2).reshape(rows, 2 * held.shape[1], block)
        bit -= 1
    return held.reshape(rows, width * block)


def halving_order(bits):
    order = [0]
    for bit in reversed(bits):
        order = [c ^ (1 << bit) for c in order] + order
    return order


def halving_sums(ratio, factor_full, contract, width, index, axis_name, bits):
    rows, factors = factor_full.shape
    block = factors // width
    order = jnp.asarray(halving_order(bits), jnp.int32) ^ index
    ordered = jnp.take(factor_full.reshape(rows, width, block), order, axis=1)
    sizes = [width >> (step + 1) for step in range(len(bits))] + [1]
    dims = (contract, ((), ()))
    terms = []
    first = 0
    for size in sizes:
        piece = ordered[:, first : first + size].reshape(rows, size * block)
        terms.append(lax.dot_general(ratio, piece, dims, preferred_element_type=jnp.float32))
        first += size
    for step, bit in enumerate(bits):
        perm = [(i, i ^ (1 << bit)) for i in range(width)]
        received = lax.ppermute(terms[step], axis_name, perm)
        offset = 0
        for later in range(step + 1, len(sizes)):
            span = terms[later].shape[1]
            terms[later] = terms[later] + received[:, offset : offset + span]
            offset += span
    return terms[-1]


def on_device(
    theta_shape,
    theta_rate,
    xi_rate,
    beta_shape,
    beta_rate,
    eta_rate,
    tile_slots,
    tile_counts,
    live_tiles,
):
    user_width = lax.axis_size("user")
    item_width = lax.axis_size("item")
    user_index = lax.axis_index("user")
    item_index = lax.axis_index("item")
    factors = theta_shape.shape[1] * item_width
    beta_columns = factors // user_width
    theta_columns = factors // item_width
    theta_part = exp_mean_log(theta_shape, theta_rate)
    beta_part = exp_mean_log(beta_shape, beta_rate)
    beta_local = jnp.sum(beta_shape / beta_rate, axis=0)
    theta_local = jnp.sum(theta_shape / theta_rate, axis=0)
    beta_placed = lax.dynamic_update_slice_in_dim(
        jnp.zeros((factors,), jnp.float32), beta_local, user_index * beta_columns, 0
    )
    theta_placed = lax.dynamic_update_slice_in_dim(
        jnp.zeros((factors,), jnp.float32), theta_local, item_index * theta_columns, 0
    )
    placed = jnp.stack([beta_placed, theta_placed])
    placed = doubling_sum(doubling_sum(placed, "item", item_width), "user", user_width)
    beta_total = placed[0]
    theta_total = placed[1]
    theta_full = doubling_gather(theta_part, "item", item_width, item_index)
    beta_full = lax.all_gather(beta_part, "user", axis=1, tiled=True)
    user_rows = theta_full.shape[0]
    item_rows = beta_full.shape[0]
    grid = dense_counts(tile_slots, tile_counts, live_tiles)
    counts = grid.transpose(0, 2, 1, 3).reshape(user_rows, item_rows).astype(jnp.float32)
    denominator = lax.dot_general(
        theta_full, beta_full, (((1,), (1,)), ((), ())), preferred_element_type=jnp.float32
    )
    ratio = (counts / denominator).astype(jnp.bfloat16)
    user_bits = list(range(user_width.bit_length() - 1))
    other_bits = user_bits[1::-1] + user_bits[2:]
    half = item_rows // 2
    item_share = jnp.concatenate(
        [
            halving_sums(
                ratio[:, :half], theta_full, ((0,), (0,)), user_width, user_index, "user",
                user_bits,
            ),
            halving_sums(
                ratio[:, half:], theta_full, ((0,), (0,)), user_width, user_index, "user",
                other_bits,
            ),
        ],
        axis=0,
    )
    xi_mean = (prior_a2 + factors * prior_a) / xi_rate
    item_bits = list(range(item_width.bit_length() - 1))
    user_share = halving_sums(
        ratio, beta_full, ((1,), (0,)), item_width, item_index, "item", item_bits
    )
    theta_shape_new = prior_a + theta_part.astype(jnp.float32) * user_share
    beta_slice = lax.dynamic_slice_in_dim(beta_total, item_index * theta_columns, theta_columns, 0)
    theta_rate_new = xi_mean[:, None] + beta_slice[None, :]
    user_part = jnp.sum(theta_shape_new / theta_rate_new, axis=1)
    xi_rate_new = prior_a2 / prior_b2 + doubling_sum(user_part, "item", item_width)
    beta_shape_new = prior_c + beta_part.astype(jnp.float32) * item_share
    eta_mean = (prior_c2 + factors * prior_c) / eta_rate
    theta_slice = lax.dynamic_slice_in_dim(theta_total, user_index * beta_columns, beta_columns, 0)
    beta_rate_new = eta_mean[:, None] + theta_slice[None, :]
    item_part = jnp.sum(beta_shape_new / beta_rate_new, axis=1)
    eta_rate_new = prior_c2 / prior_d2 + doubling_sum(item_part, "user", user_width)
    return (
        theta_shape_new,
        jnp.log(theta_rate_new),
        xi_rate_new,
        beta_shape_new,
        jnp.log(beta_rate_new),
        eta_rate_new,
    )


def solution(mesh):
    in_specs = (
        P("user", "item"),
        P("user", "item"),
        P("user"),
        P("item", "user"),
        P("item", "user"),
        P("item"),
        P("user", "item", None),
        P("user", "item", None, None, None),
        P("user", "item"),
    )
    out_specs = (
        P("user", "item"),
        P("user", "item"),
        P("user"),
        P("item", "user"),
        P("item", "user"),
        P("item"),
    )
    return jax.shard_map(
        on_device, mesh=mesh, in_specs=in_specs, out_specs=out_specs, check_vma=False
    )
```

```python
import jax
import jax.numpy as jnp
from jax import lax
from jax.sharding import PartitionSpec as P


BLK = 256
UB = 8
IB = 4
TMAX = 32


prior_a = 0.3
prior_a2 = 0.3
prior_b2 = 1.0
prior_c = 0.3
prior_c2 = 0.3
prior_d2 = 1.0


def exp_mean_log(shape_param, rate_param):
    return jnp.exp(lax.digamma(shape_param) - jnp.log(rate_param)).astype(jnp.bfloat16)


def dense_counts(tile_slots, tile_counts, live_tiles):
    slot_list = tile_slots.reshape(TMAX)
    used_slots = live_tiles.reshape(())
    positions = jnp.arange(UB * IB, dtype=jnp.int32)
    live = jnp.arange(TMAX, dtype=jnp.int32) < used_slots
    match = (slot_list[None, :] == positions[:, None]) & live[None, :]
    present = jnp.any(match, axis=1)
    source = jnp.argmax(match, axis=1)
    count_tiles = tile_counts.reshape(TMAX, BLK, BLK)
    grid = jnp.take(count_tiles, source, axis=0)
    grid = jnp.where(present[:, None, None], grid, jnp.zeros_like(grid))
    return grid.reshape(UB, IB, BLK, BLK)


def doubling_sum(value, axis_name, width):
    bit = 1
    while bit < width:
        perm = [(i, i ^ bit) for i in range(width)]
        value = value + lax.ppermute(value, axis_name, perm)
        bit *= 2
    return value


def doubling_gather(part, axis_name, width, index):
    rows, block = part.shape
    held = part.reshape(rows, 1, block)
    bit = width.bit_length() - 2
    while bit >= 0:
        partner = 1 << bit
        perm = [(i, i ^ partner) for i in range(width)]
        other = lax.ppermute(held, axis_name, perm)
        upper = ((index >> bit) & 1) == 1
        low = jnp.where(upper, other, held)
        high = jnp.where(upper, held, other)
        held = jnp.stack([low, high], axis=2).reshape(rows, 2 * held.shape[1], block)
        bit -= 1
    return held.reshape(rows, width * block)


def halving_order(bits):
    order = [0]
    for bit in reversed(bits):
        order = [c ^ (1 << bit) for c in order] + order
    return order


def halving_sums(ratio, factor_full, contract, width, index, axis_name, bits):
    rows, factors = factor_full.shape
    block = factors // width
    order = jnp.asarray(halving_order(bits), jnp.int32) ^ index
    ordered = jnp.take(factor_full.reshape(rows, width, block), order, axis=1)
    sizes = [width >> (step + 1) for step in range(len(bits))] + [1]
    dims = (contract, ((), ()))
    terms = []
    first = 0
    for size in sizes:
        piece = ordered[:, first : first + size].reshape(rows, size * block)
        terms.append(lax.dot_general(ratio, piece, dims, preferred_element_type=jnp.float32))
        first += size
    for step, bit in enumerate(bits):
        perm = [(i, i ^ (1 << bit)) for i in range(width)]
        received = lax.ppermute(terms[step], axis_name, perm)
        offset = 0
        for later in range(step + 1, len(sizes)):
            span = terms[later].shape[1]
            terms[later] = terms[later] + received[:, offset : offset + span]
            offset += span
    return terms[-1]


def on_device(
    theta_shape,
    theta_rate,
    xi_rate,
    beta_shape,
    beta_rate,
    eta_rate,
    tile_slots,
    tile_counts,
    live_tiles,
):
    user_width = lax.axis_size("user")
    item_width = lax.axis_size("item")
    user_index = lax.axis_index("user")
    item_index = lax.axis_index("item")
    factors = theta_shape.shape[1] * item_width
    beta_columns = factors // user_width
    theta_columns = factors // item_width
    beta_part = exp_mean_log(beta_shape, beta_rate)
    theta_part = exp_mean_log(theta_shape, theta_rate)
    beta_local = jnp.sum(beta_shape / beta_rate, axis=0)
    theta_local = jnp.sum(theta_shape / theta_rate, axis=0)
    beta_placed = lax.dynamic_update_slice_in_dim(
        jnp.zeros((factors,), jnp.float32), beta_local, user_index * beta_columns, 0
    )
    theta_placed = lax.dynamic_update_slice_in_dim(
        jnp.zeros((factors,), jnp.float32), theta_local, item_index * theta_columns, 0
    )
    placed = jnp.stack([beta_placed, theta_placed])
    placed = doubling_sum(doubling_sum(placed, "item", item_width), "user", user_width)
    beta_total = placed[0]
    theta_total = placed[1]
    theta_full = doubling_gather(theta_part, "item", item_width, item_index)
    beta_full = lax.all_gather(beta_part, "user", axis=1, tiled=True)
    user_rows = theta_full.shape[0]
    item_rows = beta_full.shape[0]
    grid = dense_counts(tile_slots, tile_counts, live_tiles)
    counts = grid.transpose(0, 2, 1, 3).reshape(user_rows, item_rows).astype(jnp.float32)
    denominator = lax.dot_general(
        theta_full, beta_full, (((1,), (1,)), ((), ())), preferred_element_type=jnp.float32
    )
    ratio = (counts / denominator).astype(jnp.bfloat16)
    half = item_rows // 2
    item_acc = lax.dot_general(
        ratio[:, :half], theta_full, (((0,), (0,)), ((), ())), preferred_element_type=jnp.float32
    )
    item_first = lax.psum_scatter(item_acc, "user", scatter_dimension=1, tiled=True)
    user_bits = list(range(user_width.bit_length() - 1))
    other_bits = user_bits[1::-1] + user_bits[2:]
    item_second = halving_sums(
        ratio[:, half:], theta_full, ((0,), (0,)), user_width, user_index, "user", other_bits
    )
    item_share = jnp.concatenate([item_first, item_second], axis=0)
    xi_mean = (prior_a2 + factors * prior_a) / xi_rate
    item_bits = list(range(item_width.bit_length() - 1))
    user_share = halving_sums(
        ratio, beta_full, ((1,), (0,)), item_width, item_index, "item", item_bits
    )
    theta_shape_new = prior_a + theta_part.astype(jnp.float32) * user_share
    beta_slice = lax.dynamic_slice_in_dim(beta_total, item_index * theta_columns, theta_columns, 0)
    theta_rate_new = xi_mean[:, None] + beta_slice[None, :]
    user_part = jnp.sum(theta_shape_new / theta_rate_new, axis=1)
    xi_rate_new = prior_a2 / prior_b2 + doubling_sum(user_part, "item", item_width)
    beta_shape_new = prior_c + beta_part.astype(jnp.float32) * item_share
    eta_mean = (prior_c2 + factors * prior_c) / eta_rate
    theta_slice = lax.dynamic_slice_in_dim(theta_total, user_index * beta_columns, beta_columns, 0)
    beta_rate_new = eta_mean[:, None] + theta_slice[None, :]
    item_part = jnp.sum(beta_shape_new / beta_rate_new, axis=1)
    eta_rate_new = prior_c2 / prior_d2 + doubling_sum(item_part, "user", user_width)
    return (
        theta_shape_new,
        jnp.log(theta_rate_new),
        xi_rate_new,
        beta_shape_new,
        jnp.log(beta_rate_new),
        eta_rate_new,
    )


def solution(mesh):
    in_specs = (
        P("user", "item"),
        P("user", "item"),
        P("user"),
        P("item", "user"),
        P("item", "user"),
        P("item"),
        P("user", "item", None),
        P("user", "item", None, None, None),
        P("user", "item"),
    )
    out_specs = (
        P("user", "item"),
        P("user", "item"),
        P("user"),
        P("item", "user"),
        P("item", "user"),
        P("item"),
    )
    return jax.shard_map(
        on_device, mesh=mesh, in_specs=in_specs, out_specs=out_specs, check_vma=False
    )
```

```python
import jax
import jax.numpy as jnp
from jax import lax
from jax.sharding import PartitionSpec as P


BLK = 256
UB = 8
IB = 4
TMAX = 32


prior_a = 0.3
prior_a2 = 0.3
prior_b2 = 1.0
prior_c = 0.3
prior_c2 = 0.3
prior_d2 = 1.0


def exp_mean_log(shape_param, rate_param):
    return jnp.exp(lax.digamma(shape_param) - jnp.log(rate_param)).astype(jnp.bfloat16)


def dense_counts(tile_slots, tile_counts, live_tiles):
    slot_list = tile_slots.reshape(TMAX)
    used_slots = live_tiles.reshape(())
    positions = jnp.arange(UB * IB, dtype=jnp.int32)
    live = jnp.arange(TMAX, dtype=jnp.int32) < used_slots
    match = (slot_list[None, :] == positions[:, None]) & live[None, :]
    present = jnp.any(match, axis=1)
    source = jnp.argmax(match, axis=1)
    count_tiles = tile_counts.reshape(TMAX, BLK, BLK)
    grid = jnp.take(count_tiles, source, axis=0)
    grid = jnp.where(present[:, None, None], grid, jnp.zeros_like(grid))
    return grid.reshape(UB, IB, BLK, BLK)


def doubling_sum(value, axis_name, width):
    bit = 1
    while bit < width:
        perm = [(i, i ^ bit) for i in range(width)]
        value = value + lax.ppermute(value, axis_name, perm)
        bit *= 2
    return value


def doubling_gather(part, axis_name, width, index):
    rows, block = part.shape
    held = part.reshape(rows, 1, block)
    bit = width.bit_length() - 2
    while bit >= 0:
        partner = 1 << bit
        perm = [(i, i ^ partner) for i in range(width)]
        other = lax.ppermute(held, axis_name, perm)
        upper = ((index >> bit) & 1) == 1
        low = jnp.where(upper, other, held)
        high = jnp.where(upper, held, other)
        held = jnp.stack([low, high], axis=2).reshape(rows, 2 * held.shape[1], block)
        bit -= 1
    return held.reshape(rows, width * block)


def halving_order(bits):
    order = [0]
    for bit in reversed(bits):
        order = [c ^ (1 << bit) for c in order] + order
    return order


def halving_terms(ratio, factor_full, width, index, bits):
    rows, factors = factor_full.shape
    block = factors // width
    order = jnp.asarray(halving_order(bits), jnp.int32) ^ index
    ordered = jnp.take(factor_full.reshape(rows, width, block), order, axis=1)
    sizes = [width >> (step + 1) for step in range(len(bits))] + [1]
    terms = []
    first = 0
    for size in sizes:
        piece = ordered[:, first : first + size].reshape(rows, size * block)
        terms.append(jnp.dot(ratio, piece, preferred_element_type=jnp.float32))
        first += size
    return terms


def halving_steps(terms, width, axis_name, bits):
    terms = list(terms)
    for step, bit in enumerate(bits):
        perm = [(i, i ^ (1 << bit)) for i in range(width)]
        received = lax.ppermute(terms[step], axis_name, perm)
        offset = 0
        for later in range(step + 1, len(terms)):
            span = terms[later].shape[1]
            terms[later] = terms[later] + received[:, offset : offset + span]
            offset += span
    return terms[-1]


def on_device(
    theta_shape,
    theta_rate,
    xi_rate,
    beta_shape,
    beta_rate,
    eta_rate,
    tile_slots,
    tile_counts,
    live_tiles,
):
    user_width = lax.axis_size("user")
    item_width = lax.axis_size("item")
    user_index = lax.axis_index("user")
    item_index = lax.axis_index("item")
    factors = theta_shape.shape[1] * item_width
    beta_columns = factors // user_width
    theta_columns = factors // item_width
    beta_part = exp_mean_log(beta_shape, beta_rate)
    theta_part = exp_mean_log(theta_shape, theta_rate)
    beta_local = jnp.sum(beta_shape / beta_rate, axis=0)
    theta_local = jnp.sum(theta_shape / theta_rate, axis=0)
    beta_placed = lax.dynamic_update_slice_in_dim(
        jnp.zeros((factors,), jnp.float32), beta_local, user_index * beta_columns, 0
    )
    theta_placed = lax.dynamic_update_slice_in_dim(
        jnp.zeros((factors,), jnp.float32), theta_local, item_index * theta_columns, 0
    )
    placed = jnp.stack([beta_placed, theta_placed])
    placed = doubling_sum(doubling_sum(placed, "item", item_width), "user", user_width)
    beta_total = placed[0]
    theta_total = placed[1]
    theta_full = doubling_gather(theta_part, "item", item_width, item_index)
    beta_full = lax.all_gather(beta_part, "user", axis=1, tiled=True)
    user_rows = theta_full.shape[0]
    item_rows = beta_full.shape[0]
    grid = dense_counts(tile_slots, tile_counts, live_tiles)
    counts = grid.transpose(0, 2, 1, 3).reshape(user_rows, item_rows).astype(jnp.float32)
    denominator = lax.dot_general(
        theta_full, beta_full, (((1,), (1,)), ((), ())), preferred_element_type=jnp.float32
    )
    ratio = (counts / denominator).astype(jnp.bfloat16)
    ratio_items = ratio.T
    half = item_rows // 2
    user_bits = list(range(user_width.bit_length() - 1))
    other_bits = user_bits[1::-1] + user_bits[2:]
    item_terms_a = halving_terms(ratio_items[:half], theta_full, user_width, user_index, user_bits)
    item_terms_b = halving_terms(ratio_items[half:], theta_full, user_width, user_index, other_bits)
    ratio, beta_full, item_terms_a[0], item_terms_b[0] = lax.optimization_barrier(
        (ratio, beta_full, item_terms_a[0], item_terms_b[0])
    )
    item_share = jnp.concatenate(
        [
            halving_steps(item_terms_a, user_width, "user", user_bits),
            halving_steps(item_terms_b, user_width, "user", other_bits),
        ],
        axis=0,
    )
    xi_mean = (prior_a2 + factors * prior_a) / xi_rate
    item_bits = list(range(item_width.bit_length() - 1))
    user_share = halving_steps(
        halving_terms(ratio, beta_full, item_width, item_index, item_bits),
        item_width,
        "item",
        item_bits,
    )
    theta_shape_new = prior_a + theta_part.astype(jnp.float32) * user_share
    beta_slice = lax.dynamic_slice_in_dim(beta_total, item_index * theta_columns, theta_columns, 0)
    theta_rate_new = xi_mean[:, None] + beta_slice[None, :]
    user_part = jnp.sum(theta_shape_new / theta_rate_new, axis=1)
    xi_rate_new = prior_a2 / prior_b2 + doubling_sum(user_part, "item", item_width)
    beta_shape_new = prior_c + beta_part.astype(jnp.float32) * item_share
    eta_mean = (prior_c2 + factors * prior_c) / eta_rate
    theta_slice = lax.dynamic_slice_in_dim(theta_total, user_index * beta_columns, beta_columns, 0)
    beta_rate_new = eta_mean[:, None] + theta_slice[None, :]
    item_part = jnp.sum(beta_shape_new / beta_rate_new, axis=1)
    eta_rate_new = prior_c2 / prior_d2 + doubling_sum(item_part, "user", user_width)
    return (
        theta_shape_new,
        jnp.log(theta_rate_new),
        xi_rate_new,
        beta_shape_new,
        jnp.log(beta_rate_new),
        eta_rate_new,
    )


def solution(mesh):
    in_specs = (
        P("user", "item"),
        P("user", "item"),
        P("user"),
        P("item", "user"),
        P("item", "user"),
        P("item"),
        P("user", "item", None),
        P("user", "item", None, None, None),
        P("user", "item"),
    )
    out_specs = (
        P("user", "item"),
        P("user", "item"),
        P("user"),
        P("item", "user"),
        P("item", "user"),
        P("item"),
    )
    return jax.shard_map(
        on_device, mesh=mesh, in_specs=in_specs, out_specs=out_specs, check_vma=False
    )
```

```python
import jax
import jax.numpy as jnp
from jax import lax
from jax.sharding import PartitionSpec as P


BLK = 256
UB = 8
IB = 4
TMAX = 32


prior_a = 0.3
prior_a2 = 0.3
prior_b2 = 1.0
prior_c = 0.3
prior_c2 = 0.3
prior_d2 = 1.0


def exp_mean_log(shape_param, rate_param):
    return jnp.exp(lax.digamma(shape_param) - jnp.log(rate_param)).astype(jnp.bfloat16)


def dense_counts(tile_slots, tile_counts, live_tiles):
    slot_list = tile_slots.reshape(TMAX)
    used_slots = live_tiles.reshape(())
    positions = jnp.arange(UB * IB, dtype=jnp.int32)
    live = jnp.arange(TMAX, dtype=jnp.int32) < used_slots
    match = (slot_list[None, :] == positions[:, None]) & live[None, :]
    present = jnp.any(match, axis=1)
    source = jnp.argmax(match, axis=1)
    count_tiles = tile_counts.reshape(TMAX, BLK, BLK)
    grid = jnp.take(count_tiles, source, axis=0)
    grid = jnp.where(present[:, None, None], grid, jnp.zeros_like(grid))
    return grid.reshape(UB, IB, BLK, BLK)


def doubling_sum(value, axis_name, width):
    bit = 1
    while bit < width:
        perm = [(i, i ^ bit) for i in range(width)]
        value = value + lax.ppermute(value, axis_name, perm)
        bit *= 2
    return value


def doubling_gather(part, axis_name, width, index):
    rows, block = part.shape
    held = part.reshape(rows, 1, block)
    bit = width.bit_length() - 2
    while bit >= 0:
        partner = 1 << bit
        perm = [(i, i ^ partner) for i in range(width)]
        other = lax.ppermute(held, axis_name, perm)
        upper = ((index >> bit) & 1) == 1
        low = jnp.where(upper, other, held)
        high = jnp.where(upper, held, other)
        held = jnp.stack([low, high], axis=2).reshape(rows, 2 * held.shape[1], block)
        bit -= 1
    return held.reshape(rows, width * block)


def halving_order(width):
    order = [0]
    step = width
    while step > 1:
        step //= 2
        order = [c ^ step for c in order] + order
    return order


def halving_user_sums(ratio, beta_full, width, index, axis_name):
    items, factors = beta_full.shape
    block = factors // width
    order = jnp.asarray(halving_order(width), jnp.int32) ^ index
    beta_ordered = jnp.take(beta_full.reshape(items, width, block), order, axis=1)
    sizes = []
    size = width
    while size > 1:
        size //= 2
        sizes.append(size)
    sizes.append(1)
    terms = []
    first = 0
    for size in sizes:
        piece = beta_ordered[:, first : first + size].reshape(items, size * block)
        terms.append(jnp.dot(ratio, piece, preferred_element_type=jnp.float32))
        first += size
    for step_index in range(len(sizes) - 1):
        partner = 1 << step_index
        perm = [(i, i ^ partner) for i in range(width)]
        received = lax.ppermute(terms[step_index], axis_name, perm)
        offset = 0
        for later in range(step_index + 1, len(sizes)):
            span = terms[later].shape[1]
            terms[later] = terms[later] + received[:, offset : offset + span]
            offset += span
    return terms[-1]


def on_device(
    theta_shape,
    theta_rate,
    xi_rate,
    beta_shape,
    beta_rate,
    eta_rate,
    tile_slots,
    tile_counts,
    live_tiles,
):
    user_width = lax.axis_size("user")
    item_width = lax.axis_size("item")
    user_index = lax.axis_index("user")
    item_index = lax.axis_index("item")
    factors = theta_shape.shape[1] * item_width
    beta_columns = factors // user_width
    theta_columns = factors // item_width
    beta_part = exp_mean_log(beta_shape, beta_rate)
    theta_part = exp_mean_log(theta_shape, theta_rate)
    beta_local = jnp.sum(beta_shape / beta_rate, axis=0)
    theta_local = jnp.sum(theta_shape / theta_rate, axis=0)
    beta_placed = lax.dynamic_update_slice_in_dim(
        jnp.zeros((factors,), jnp.float32), beta_local, user_index * beta_columns, 0
    )
    theta_placed = lax.dynamic_update_slice_in_dim(
        jnp.zeros((factors,), jnp.float32), theta_local, item_index * theta_columns, 0
    )
    placed = jnp.stack([beta_placed, theta_placed])
    theta_full = doubling_gather(theta_part, "item", item_width, item_index)
    beta_full = lax.all_gather(beta_part, "user", axis=1, tiled=True)
    user_rows = theta_full.shape[0]
    item_rows = beta_full.shape[0]
    placed, beta_full = lax.optimization_barrier((placed, beta_full))
    placed = doubling_sum(doubling_sum(placed, "item", item_width), "user", user_width)
    beta_total = placed[0]
    theta_total = placed[1]
    grid = dense_counts(tile_slots, tile_counts, live_tiles)
    counts = grid.transpose(0, 2, 1, 3).reshape(user_rows, item_rows).astype(jnp.float32)
    denominator = lax.dot_general(
        theta_full, beta_full, (((1,), (1,)), ((), ())), preferred_element_type=jnp.float32
    )
    ratio = (counts / denominator).astype(jnp.bfloat16)
    item_acc = lax.dot_general(
        ratio, theta_full, (((0,), (0,)), ((), ())), preferred_element_type=jnp.float32
    )
    xi_mean = (prior_a2 + factors * prior_a) / xi_rate
    user_share = halving_user_sums(ratio, beta_full, item_width, item_index, "item")
    theta_shape_new = prior_a + theta_part.astype(jnp.float32) * user_share
    beta_slice = lax.dynamic_slice_in_dim(beta_total, item_index * theta_columns, theta_columns, 0)
    theta_rate_new = xi_mean[:, None] + beta_slice[None, :]
    user_part = jnp.sum(theta_shape_new / theta_rate_new, axis=1)
    xi_rate_new = prior_a2 / prior_b2 + doubling_sum(user_part, "item", item_width)
    item_share = lax.psum_scatter(item_acc, "user", scatter_dimension=1, tiled=True)
    beta_shape_new = prior_c + beta_part.astype(jnp.float32) * item_share
    eta_mean = (prior_c2 + factors * prior_c) / eta_rate
    theta_slice = lax.dynamic_slice_in_dim(theta_total, user_index * beta_columns, beta_columns, 0)
    beta_rate_new = eta_mean[:, None] + theta_slice[None, :]
    rate_every = eta_mean[:, None] + theta_total[None, :]
    prior_part = jnp.sum(prior_c / rate_every, axis=1)
    device_part = jnp.sum(beta_full.astype(jnp.float32) / rate_every * item_acc, axis=1)
    eta_rate_new = prior_c2 / prior_d2 + (prior_part + doubling_sum(device_part, "user", user_width))
    return (
        theta_shape_new,
        jnp.log(theta_rate_new),
        xi_rate_new,
        beta_shape_new,
        jnp.log(beta_rate_new),
        eta_rate_new,
    )


def solution(mesh):
    in_specs = (
        P("user", "item"),
        P("user", "item"),
        P("user"),
        P("item", "user"),
        P("item", "user"),
        P("item"),
        P("user", "item", None),
        P("user", "item", None, None, None),
        P("user", "item"),
    )
    out_specs = (
        P("user", "item"),
        P("user", "item"),
        P("user"),
        P("item", "user"),
        P("item", "user"),
        P("item"),
    )
    return jax.shard_map(
        on_device, mesh=mesh, in_specs=in_specs, out_specs=out_specs, check_vma=False
    )
```

```python
import jax
import jax.numpy as jnp
from jax import lax
from jax.sharding import PartitionSpec as P


BLK = 256
UB = 8
IB = 4
TMAX = 32


prior_a = 0.3
prior_a2 = 0.3
prior_b2 = 1.0
prior_c = 0.3
prior_c2 = 0.3
prior_d2 = 1.0


def exp_mean_log(shape_param, rate_param):
    return jnp.exp(lax.digamma(shape_param) - jnp.log(rate_param)).astype(jnp.bfloat16)


def dense_counts(tile_slots, tile_counts, live_tiles):
    slot_list = tile_slots.reshape(TMAX)
    used_slots = live_tiles.reshape(())
    positions = jnp.arange(UB * IB, dtype=jnp.int32)
    live = jnp.arange(TMAX, dtype=jnp.int32) < used_slots
    match = (slot_list[None, :] == positions[:, None]) & live[None, :]
    present = jnp.any(match, axis=1)
    source = jnp.argmax(match, axis=1)
    count_tiles = tile_counts.reshape(TMAX, BLK, BLK)
    grid = jnp.take(count_tiles, source, axis=0)
    grid = jnp.where(present[:, None, None], grid, jnp.zeros_like(grid))
    return grid.reshape(UB, IB, BLK, BLK)


def doubling_sum(value, axis_name, width):
    bit = 1
    while bit < width:
        perm = [(i, i ^ bit) for i in range(width)]
        value = value + lax.ppermute(value, axis_name, perm)
        bit *= 2
    return value


def doubling_gather(part, axis_name, width, index):
    rows, block = part.shape
    held = part.reshape(rows, 1, block)
    bit = width.bit_length() - 2
    while bit >= 0:
        partner = 1 << bit
        perm = [(i, i ^ partner) for i in range(width)]
        other = lax.ppermute(held, axis_name, perm)
        upper = ((index >> bit) & 1) == 1
        low = jnp.where(upper, other, held)
        high = jnp.where(upper, held, other)
        held = jnp.stack([low, high], axis=2).reshape(rows, 2 * held.shape[1], block)
        bit -= 1
    return held.reshape(rows, width * block)


def halving_order(width):
    order = [0]
    step = width
    while step > 1:
        step //= 2
        order = [c ^ step for c in order] + order
    return order


def halving_user_sums(ratio, beta_full, width, index, axis_name):
    items, factors = beta_full.shape
    block = factors // width
    order = jnp.asarray(halving_order(width), jnp.int32) ^ index
    beta_ordered = jnp.take(beta_full.reshape(items, width, block), order, axis=1)
    sizes = []
    size = width
    while size > 1:
        size //= 2
        sizes.append(size)
    sizes.append(1)
    terms = []
    first = 0
    for size in sizes:
        piece = beta_ordered[:, first : first + size].reshape(items, size * block)
        terms.append(jnp.dot(ratio, piece, preferred_element_type=jnp.float32))
        first += size
    for step_index in range(len(sizes) - 1):
        partner = 1 << step_index
        perm = [(i, i ^ partner) for i in range(width)]
        received = lax.ppermute(terms[step_index], axis_name, perm)
        offset = 0
        for later in range(step_index + 1, len(sizes)):
            span = terms[later].shape[1]
            terms[later] = terms[later] + received[:, offset : offset + span]
            offset += span
    return terms[-1]


def on_device(
    theta_shape,
    theta_rate,
    xi_rate,
    beta_shape,
    beta_rate,
    eta_rate,
    tile_slots,
    tile_counts,
    live_tiles,
):
    user_width = lax.axis_size("user")
    item_width = lax.axis_size("item")
    user_index = lax.axis_index("user")
    item_index = lax.axis_index("item")
    factors = theta_shape.shape[1] * item_width
    beta_columns = factors // user_width
    theta_columns = factors // item_width
    beta_part = exp_mean_log(beta_shape, beta_rate)
    theta_part = exp_mean_log(theta_shape, theta_rate)
    beta_local = jnp.sum(beta_shape / beta_rate, axis=0)
    theta_local = jnp.sum(theta_shape / theta_rate, axis=0)
    beta_placed = lax.dynamic_update_slice_in_dim(
        jnp.zeros((factors,), jnp.float32), beta_local, user_index * beta_columns, 0
    )
    theta_placed = lax.dynamic_update_slice_in_dim(
        jnp.zeros((factors,), jnp.float32), theta_local, item_index * theta_columns, 0
    )
    placed = jnp.stack([beta_placed, theta_placed])
    theta_full = doubling_gather(theta_part, "item", item_width, item_index)
    beta_full = lax.all_gather(beta_part, "user", axis=1, tiled=True)
    user_rows = theta_full.shape[0]
    item_rows = beta_full.shape[0]
    grid = dense_counts(tile_slots, tile_counts, live_tiles)
    grid = grid.transpose(0, 2, 1, 3).reshape(user_rows, item_rows)
    placed, beta_full, grid = lax.optimization_barrier((placed, beta_full, grid))
    placed = doubling_sum(doubling_sum(placed, "item", item_width), "user", user_width)
    beta_total = placed[0]
    theta_total = placed[1]
    counts = grid.astype(jnp.float32)
    denominator = lax.dot_general(
        theta_full, beta_full, (((1,), (1,)), ((), ())), preferred_element_type=jnp.float32
    )
    ratio = (counts / denominator).astype(jnp.bfloat16)
    item_acc = lax.dot_general(
        ratio, theta_full, (((0,), (0,)), ((), ())), preferred_element_type=jnp.float32
    )
    xi_mean = (prior_a2 + factors * prior_a) / xi_rate
    user_share = halving_user_sums(ratio, beta_full, item_width, item_index, "item")
    theta_shape_new = prior_a + theta_part.astype(jnp.float32) * user_share
    beta_slice = lax.dynamic_slice_in_dim(beta_total, item_index * theta_columns, theta_columns, 0)
    theta_rate_new = xi_mean[:, None] + beta_slice[None, :]
    user_part = jnp.sum(theta_shape_new / theta_rate_new, axis=1)
    xi_rate_new = prior_a2 / prior_b2 + doubling_sum(user_part, "item", item_width)
    item_share = lax.psum_scatter(item_acc, "user", scatter_dimension=1, tiled=True)
    beta_shape_new = prior_c + beta_part.astype(jnp.float32) * item_share
    eta_mean = (prior_c2 + factors * prior_c) / eta_rate
    theta_slice = lax.dynamic_slice_in_dim(theta_total, user_index * beta_columns, beta_columns, 0)
    beta_rate_new = eta_mean[:, None] + theta_slice[None, :]
    rate_every = eta_mean[:, None] + theta_total[None, :]
    prior_part = jnp.sum(prior_c / rate_every, axis=1)
    device_part = jnp.sum(
        beta_full.astype(jnp.float32) / rate_every * lax.optimization_barrier(item_acc), axis=1
    )
    eta_rate_new = prior_c2 / prior_d2 + (prior_part + doubling_sum(device_part, "user", user_width))
    return (
        theta_shape_new,
        jnp.log(theta_rate_new),
        xi_rate_new,
        beta_shape_new,
        jnp.log(beta_rate_new),
        eta_rate_new,
    )


def solution(mesh):
    in_specs = (
        P("user", "item"),
        P("user", "item"),
        P("user"),
        P("item", "user"),
        P("item", "user"),
        P("item"),
        P("user", "item", None),
        P("user", "item", None, None, None),
        P("user", "item"),
    )
    out_specs = (
        P("user", "item"),
        P("user", "item"),
        P("user"),
        P("item", "user"),
        P("item", "user"),
        P("item"),
    )
    return jax.shard_map(
        on_device, mesh=mesh, in_specs=in_specs, out_specs=out_specs, check_vma=False
    )
```
